256 devices in a mesh: outer: 32 (over z, x), inner: 8 (over y, core).
Axes of the slice: x: 4, y: 4, z: 8, core: 2. Of those that a mesh axis runs over, the one named last changes fastest.
Arguments:
- queries: bfloat16 [262144, 1024], P(('outer', 'inner')), may hold values from -6 to 6
- keys: bfloat16 [262144, 1024], P(('outer', 'inner')), may hold values from -6 to 6
- values: bfloat16 [262144, 1024], P(('outer', 'inner')), may hold values from -6 to 6
- norm_gain: float32 [1024], replicated, may hold values from 0.1 to 1.9
- out_weight: bfloat16 [1024, 2048], replicated, may hold values from -0.1875 to 0.1875
Outputs:
- mixed: bfloat16 [262144, 2048], P(('outer', 'inner'))
The draws below stay inside these ranges and needn't reach their ends.
All inputs are finite; a program needn't handle non-finite values.
Results may differ from the reference program's by a relative error of at most 0.0058.
Values sent between devices are 32-bit elements; how exact they have to be, the bound alone decides.
No kernel may reach another device: no remote copies, remote signals or barrier semaphores. Data moves between devices by JAX's collectives and lax.ppermute only.
A program may use at most 320 MiB of HBM per device.

```python
import jax
import jax.numpy as jnp
from jax import lax

D = 2048
H = 8
DH = 128
C = 128
TOK_DEV = 1024
HD = 1024
TOKENS = 262144


def level_of(rng, shape, split, low, high):
    level, own = 1.0, jax.random.fold_in(rng, 6)
    for dim, parts in split:
        heights = jnp.exp(jax.random.uniform(jax.random.fold_in(own, dim), (parts,), jnp.float32, low / len(split), high / len(split)))
        level = level * jnp.repeat(heights, shape[dim] // parts).reshape([-1 if axis == dim else 1 for axis in range(len(shape))])
    return level


def bell_draw(own_key, extent, deviation, bound, pieces=(), kind=jnp.bfloat16):
    result = jax.random.normal(own_key, extent, jnp.float32) * deviation
    if len(pieces) > 0:
        result = level_of(own_key, extent, pieces, -0.22, 0.18) * result
    return jnp.clip(result, min=-bound, max=bound).astype(kind)


def setup_inputs(seed: int = 0) -> dict:
    arg_keys = jax.random.split(jax.random.key(seed), 6)
    return {
        "queries": bell_draw(arg_keys[0], (TOKENS, HD), 1.0, 6.0, ((0, 256),)),
        "keys": bell_draw(arg_keys[1], (TOKENS, HD), 1.0, 6.0, ((0, 256),)),
        "values": bell_draw(arg_keys[2], (TOKENS, HD), 1.0, 6.0, ((0, 256),)),
        "norm_gain": jnp.clip(1.0 + 0.18 * jax.random.normal(arg_keys[3], (HD,), jnp.float32), 0.1, 1.9),
        "out_weight": bell_draw(arg_keys[4], (HD, D), HD ** -0.5, 0.1875),
    }


def block_step(carried, inputs):
    query_rows, key_rows, value_rows, norm_gain, out_weight = inputs
    blocks = TOK_DEV // C
    query_blocks = query_rows.reshape(blocks, C, H, DH).astype(jnp.float32)
    key_blocks = key_rows.reshape(blocks, C, H, DH).astype(jnp.float32)
    value_blocks = value_rows.reshape(blocks, C, H, DH).astype(jnp.float32)
    states = jnp.einsum('nchd,nche->nhde', key_blocks, value_blocks)
    running = jnp.cumsum(states, axis=0)
    within = jnp.concatenate([jnp.zeros_like(carried)[None], running[:-1]], axis=0)
    prefix_low = (carried[None] + within).astype(jnp.bfloat16)
    scores = jnp.einsum('nchd,nshd->nhcs', query_blocks, key_blocks)
    causal = jnp.arange(C)[:, None] >= jnp.arange(C)[None, :]
    weights = jnp.where(causal[None, None], scores, 0.0).astype(jnp.bfloat16)
    inside = jnp.einsum('nhcs,nshd->nchd', weights.astype(jnp.float32), value_blocks)
    carried_term = jnp.einsum('nchd,nhde->nche', query_blocks, prefix_low.astype(jnp.float32))
    attended = inside + carried_term
    mean_square = lax.optimization_barrier(jnp.mean(attended * attended, axis=-1, keepdims=True))
    normed = attended * lax.rsqrt(mean_square + 1e-06) * norm_gain.reshape(H, DH)
    normed = normed.astype(jnp.bfloat16).reshape(TOK_DEV, H * DH)
    mixed = jnp.dot(normed, out_weight, preferred_element_type=jnp.float32).astype(jnp.bfloat16)
    return (carried + lax.optimization_barrier(jnp.sum(states, axis=0)), mixed)

def reference(queries, keys, values, norm_gain, out_weight):
    count = TOKENS // TOK_DEV
    width = H * DH
    query_all = queries.reshape(count, TOK_DEV, width)
    key_all = keys.reshape(count, TOK_DEV, width)
    value_all = values.reshape(count, TOK_DEV, width)

    def step(carried, trio):
        return block_step(carried, (trio[0], trio[1], trio[2], norm_gain, out_weight))
    start_state = jnp.zeros((H, DH, DH), jnp.float32)
    final_state, mixed = lax.scan(step, start_state, (query_all, key_all, value_all))
    return mixed.reshape(TOKENS, D)
```

```python
import jax
import jax.numpy as jnp
from jax import lax
from jax.sharding import PartitionSpec as P

H = 8
DH = 128
C = 128


def exclusive_cumsum(rows):
    running = jnp.cumsum(rows, axis=0)
    return jnp.concatenate([jnp.zeros_like(rows[:1]), running[:-1]], axis=0), running[-1]


def carried_state(local_total):
    n_inner = lax.axis_size("inner")
    n_outer = lax.axis_size("outer")
    size = local_total.size
    chunks = local_total.reshape(n_inner, size // n_inner)
    gathered = lax.all_to_all(chunks, "inner", 0, 0, tiled=True)
    inner_before, group_total = exclusive_cumsum(gathered)
    pieces = lax.all_to_all(group_total.reshape(n_outer, -1), "outer", 0, 0, tiled=True)
    outer_before, _ = exclusive_cumsum(pieces)
    outer_chunk = lax.all_to_all(outer_before, "outer", 0, 0, tiled=True).reshape(-1)
    summed = inner_before + outer_chunk[None, :]
    back = lax.all_to_all(summed, "inner", 0, 0, tiled=True)
    return back.reshape(local_total.shape)


def on_device(queries, keys, values, norm_gain, out_weight):
    tok_rows = queries.shape[0]
    blocks = tok_rows // C
    query_blocks = queries.reshape(blocks, C, H, DH)
    key_blocks = keys.reshape(blocks, C, H, DH)
    value_blocks = values.reshape(blocks, C, H, DH)
    states = jnp.einsum(
        "nchd,nche->nhde", key_blocks, value_blocks, preferred_element_type=jnp.float32
    )
    local_total = jnp.sum(states, axis=0)
    running = jnp.cumsum(states, axis=0)
    empty_state = jnp.zeros_like(local_total)
    within = jnp.concatenate([empty_state[None], running[:-1]], axis=0)
    scores = jnp.einsum(
        "nchd,nshd->nhcs", query_blocks, key_blocks, preferred_element_type=jnp.float32
    )
    causal = lax.broadcasted_iota(jnp.int32, (C, C), 0) >= lax.broadcasted_iota(
        jnp.int32, (C, C), 1
    )
    weights = jnp.where(causal[None, None], scores, 0.0).astype(jnp.bfloat16)
    inside = jnp.einsum(
        "nhcs,nshd->nchd", weights, value_blocks, preferred_element_type=jnp.float32
    )
    carried = carried_state(local_total)
    prefix_low = (carried[None] + within).astype(jnp.bfloat16)
    carried_term = jnp.einsum(
        "nchd,nhde->nche", query_blocks, prefix_low, preferred_element_type=jnp.float32
    )
    attended = inside + carried_term
    mean_square = jnp.mean(attended * attended, axis=-1, keepdims=True)
    normed = attended * lax.rsqrt(mean_square + 1e-06) * norm_gain.reshape(H, DH)
    normed = normed.astype(jnp.bfloat16).reshape(tok_rows, H * DH)
    return jnp.dot(normed, out_weight, preferred_element_type=jnp.float32).astype(jnp.bfloat16)


def solution(mesh):
    return jax.shard_map(
        on_device,
        mesh=mesh,
        in_specs=(
            P(("outer", "inner"), None),
            P(("outer", "inner"), None),
            P(("outer", "inner"), None),
            P(),
            P(),
        ),
        out_specs=P(("outer", "inner"), None),
        check_vma=False,
    )
```

```python
import jax
import jax.numpy as jnp
from jax import lax
from jax.experimental import pallas as pl
from jax.experimental.pallas import tpu as pltpu
from jax.sharding import PartitionSpec as P

H = 8
DH = 128
C = 128


def exclusive_cumsum(rows):
    running = jnp.cumsum(rows, axis=0)
    return jnp.concatenate([jnp.zeros_like(rows[:1]), running[:-1]], axis=0), running[-1]


def carried_state(local_total):
    n_inner = lax.axis_size("inner")
    n_outer = lax.axis_size("outer")
    size = local_total.size
    chunks = local_total.reshape(n_inner, size // n_inner)
    gathered = lax.all_to_all(chunks, "inner", 0, 0, tiled=True)
    inner_before, group_total = exclusive_cumsum(gathered)
    pieces = lax.all_to_all(group_total.reshape(n_outer, -1), "outer", 0, 0, tiled=True)
    outer_before, _ = exclusive_cumsum(pieces)
    outer_chunk = lax.all_to_all(outer_before, "outer", 0, 0, tiled=True).reshape(-1)
    summed = inner_before + outer_chunk[None, :]
    back = lax.all_to_all(summed, "inner", 0, 0, tiled=True)
    return back.reshape(local_total.shape)


TILE = 256


def state_kernel(k_ref, v_ref, out_ref):
    for h in range(H):
        cols = slice(h * DH, (h + 1) * DH)
        out_ref[h] = lax.dot_general(
            k_ref[:, cols], v_ref[:, cols], (((0,), (0,)), ((), ())),
            preferred_element_type=jnp.float32,
        )


def state_totals(keys, values):
    rows = keys.shape[0]
    return pl.pallas_call(
        state_kernel,
        out_shape=jax.ShapeDtypeStruct((H, DH, DH), jnp.float32),
        grid=(1,),
        in_specs=[
            pl.BlockSpec((rows, H * DH), lambda i: (0, 0)),
            pl.BlockSpec((rows, H * DH), lambda i: (0, 0)),
        ],
        out_specs=pl.BlockSpec((H, DH, DH), lambda i: (0, 0, 0)),
    )(keys, values)


def layer_kernel(q_ref, k_ref, v_ref, c_ref, g_ref, w_ref, o_ref, run_ref, n_ref):
    @pl.when(pl.program_id(0) == 0)
    def _():
        run_ref[...] = c_ref[...]

    causal = lax.broadcasted_iota(jnp.int32, (C, C), 0) >= lax.broadcasted_iota(jnp.int32, (C, C), 1)
    for b in range(TILE // C):
        rows = slice(b * C, (b + 1) * C)
        for h in range(H):
            cols = slice(h * DH, (h + 1) * DH)
            qb = q_ref[rows, cols]
            kb = k_ref[rows, cols]
            vb = v_ref[rows, cols]
            scores = lax.dot_general(
                qb, kb, (((1,), (1,)), ((), ())), preferred_element_type=jnp.float32
            )
            weights = jnp.where(causal, scores, 0.0).astype(jnp.bfloat16)
            inside = jnp.dot(weights, vb, preferred_element_type=jnp.float32)
            prev = run_ref[h]
            carried_term = jnp.dot(qb, prev.astype(jnp.bfloat16), preferred_element_type=jnp.float32)
            attended = inside + carried_term
            mean_square = jnp.mean(attended * attended, axis=-1, keepdims=True)
            normed = attended * lax.rsqrt(mean_square + 1e-06) * g_ref[:, cols]
            n_ref[rows, cols] = normed.astype(jnp.bfloat16)
            run_ref[h] = prev + lax.dot_general(
                kb, vb, (((0,), (0,)), ((), ())), preferred_element_type=jnp.float32
            )
    o_ref[...] = jnp.dot(n_ref[...], w_ref[...], preferred_element_type=jnp.float32).astype(
        jnp.bfloat16
    )


def layer(queries, keys, values, carried, norm_gain, out_weight):
    rows, width = queries.shape
    out_width = out_weight.shape[1]
    tok = lambda t: (t, 0)
    fixed2 = lambda t: (0, 0)
    return pl.pallas_call(
        layer_kernel,
        out_shape=jax.ShapeDtypeStruct((rows, out_width), jnp.bfloat16),
        grid=(rows // TILE,),
        in_specs=[
            pl.BlockSpec((TILE, width), tok),
            pl.BlockSpec((TILE, width), tok),
            pl.BlockSpec((TILE, width), tok),
            pl.BlockSpec((H, DH, DH), lambda t: (0, 0, 0)),
            pl.BlockSpec((1, width), fixed2),
            pl.BlockSpec((width, out_width), fixed2),
        ],
        out_specs=pl.BlockSpec((TILE, out_width), tok),
        scratch_shapes=[
            pltpu.VMEM((H, DH, DH), jnp.float32),
            pltpu.VMEM((TILE, width), jnp.bfloat16),
        ],
        compiler_params=pltpu.CompilerParams(dimension_semantics=("arbitrary",)),
    )(queries, keys, values, carried, norm_gain.reshape(1, width), out_weight)


def on_device(queries, keys, values, norm_gain, out_weight):
    local_total = state_totals(keys, values)
    carried = carried_state(local_total)
    return layer(queries, keys, values, carried, norm_gain, out_weight)


def solution(mesh):
    return jax.shard_map(
        on_device,
        mesh=mesh,
        in_specs=(
            P(("outer", "inner"), None),
            P(("outer", "inner"), None),
            P(("outer", "inner"), None),
            P(),
            P(),
        ),
        out_specs=P(("outer", "inner"), None),
        check_vma=False,
    )
```

```python
import jax
import jax.numpy as jnp
from jax import lax
from jax.experimental import pallas as pl
from jax.experimental.pallas import tpu as pltpu
from jax.sharding import PartitionSpec as P

H = 8
DH = 128
C = 128


def exclusive_cumsum(rows):
    running = jnp.cumsum(rows, axis=0)
    return jnp.concatenate([jnp.zeros_like(rows[:1]), running[:-1]], axis=0), running[-1]


def carried_state(local_total):
    n_inner = lax.axis_size("inner")
    n_outer = lax.axis_size("outer")
    size = local_total.size
    chunks = local_total.reshape(n_inner, size // n_inner)
    gathered = lax.all_to_all(chunks, "inner", 0, 0, tiled=True)
    inner_before, group_total = exclusive_cumsum(gathered)
    pieces = lax.all_to_all(group_total.reshape(n_outer, -1), "outer", 0, 0, tiled=True)
    outer_before, _ = exclusive_cumsum(pieces)
    outer_chunk = lax.all_to_all(outer_before, "outer", 0, 0, tiled=True).reshape(-1)
    summed = inner_before + outer_chunk[None, :]
    back = lax.all_to_all(summed, "inner", 0, 0, tiled=True)
    return back.reshape(local_total.shape)


TILE = 256


def state_kernel(k_ref, v_ref, out_ref):
    @pl.when(pl.program_id(0) == 0)
    def _():
        out_ref[...] = jnp.zeros_like(out_ref)

    for h in range(H):
        cols = slice(h * DH, (h + 1) * DH)
        out_ref[h] += lax.dot_general(
            k_ref[:, cols], v_ref[:, cols], (((0,), (0,)), ((), ())),
            preferred_element_type=jnp.float32,
        )


def state_totals(keys, values):
    rows, width = keys.shape
    return pl.pallas_call(
        state_kernel,
        out_shape=jax.ShapeDtypeStruct((H, DH, DH), jnp.float32),
        grid=(rows // TILE,),
        in_specs=[
            pl.BlockSpec((TILE, width), lambda t: (t, 0)),
            pl.BlockSpec((TILE, width), lambda t: (t, 0)),
        ],
        out_specs=pl.BlockSpec((H, DH, DH), lambda t: (0, 0, 0)),
        compiler_params=pltpu.CompilerParams(dimension_semantics=("arbitrary",)),
    )(keys, values)


def intra_kernel(q_ref, k_ref, v_ref, out_ref):
    causal = lax.broadcasted_iota(jnp.int32, (C, C), 0) >= lax.broadcasted_iota(jnp.int32, (C, C), 1)
    for b in range(TILE // C):
        rows = slice(b * C, (b + 1) * C)
        for h in range(H):
            cols = slice(h * DH, (h + 1) * DH)
            vb = v_ref[rows, cols]
            scores = lax.dot_general(
                q_ref[rows, cols], k_ref[rows, cols], (((1,), (1,)), ((), ())),
                preferred_element_type=jnp.float32,
            )
            weights = jnp.where(causal, scores, 0.0).astype(jnp.bfloat16)
            out_ref[rows, cols] = jnp.dot(weights, vb, preferred_element_type=jnp.float32)


def intra_block(queries, keys, values):
    rows, width = queries.shape
    tok = lambda t: (t, 0)
    return pl.pallas_call(
        intra_kernel,
        out_shape=jax.ShapeDtypeStruct((rows, width), jnp.float32),
        grid=(rows // TILE,),
        in_specs=[pl.BlockSpec((TILE, width), tok)] * 3,
        out_specs=pl.BlockSpec((TILE, width), tok),
    )(queries, keys, values)


def layer_kernel(q_ref, k_ref, v_ref, i_ref, c_ref, g_ref, w_ref, o_ref, run_ref, n_ref):
    @pl.when(pl.program_id(0) == 0)
    def _():
        run_ref[...] = c_ref[...]

    for b in range(TILE // C):
        rows = slice(b * C, (b + 1) * C)
        for h in range(H):
            cols = slice(h * DH, (h + 1) * DH)
            qb = q_ref[rows, cols]
            prev = run_ref[h]
            carried_term = jnp.dot(qb, prev.astype(jnp.bfloat16), preferred_element_type=jnp.float32)
            attended = i_ref[rows, cols] + carried_term
            mean_square = jnp.mean(attended * attended, axis=-1, keepdims=True)
            normed = attended * lax.rsqrt(mean_square + 1e-06) * g_ref[:, cols]
            n_ref[rows, cols] = normed.astype(jnp.bfloat16)
            run_ref[h] = prev + lax.dot_general(
                k_ref[rows, cols], v_ref[rows, cols], (((0,), (0,)), ((), ())),
                preferred_element_type=jnp.float32,
            )
    o_ref[...] = jnp.dot(n_ref[...], w_ref[...], preferred_element_type=jnp.float32).astype(
        jnp.bfloat16
    )


def layer(queries, keys, values, inside, carried, norm_gain, out_weight):
    rows, width = queries.shape
    out_width = out_weight.shape[1]
    tok = lambda t: (t, 0)
    fixed2 = lambda t: (0, 0)
    return pl.pallas_call(
        layer_kernel,
        out_shape=jax.ShapeDtypeStruct((rows, out_width), jnp.bfloat16),
        grid=(rows // TILE,),
        in_specs=[
            pl.BlockSpec((TILE, width), tok),
            pl.BlockSpec((TILE, width), tok),
            pl.BlockSpec((TILE, width), tok),
            pl.BlockSpec((TILE, width), tok),
            pl.BlockSpec((H, DH, DH), lambda t: (0, 0, 0)),
            pl.BlockSpec((1, width), fixed2),
            pl.BlockSpec((width, out_width), fixed2),
        ],
        out_specs=pl.BlockSpec((TILE, out_width), tok),
        scratch_shapes=[
            pltpu.VMEM((H, DH, DH), jnp.float32),
            pltpu.VMEM((TILE, width), jnp.bfloat16),
        ],
        compiler_params=pltpu.CompilerParams(dimension_semantics=("arbitrary",)),
    )(queries, keys, values, inside, carried, norm_gain.reshape(1, width), out_weight)


def on_device(queries, keys, values, norm_gain, out_weight):
    local_total = state_totals(keys, values)
    inside = intra_block(queries, keys, values)
    carried = carried_state(local_total)
    return layer(queries, keys, values, inside, carried, norm_gain, out_weight)


def solution(mesh):
    return jax.shard_map(
        on_device,
        mesh=mesh,
        in_specs=(
            P(("outer", "inner"), None),
            P(("outer", "inner"), None),
            P(("outer", "inner"), None),
            P(),
            P(),
        ),
        out_specs=P(("outer", "inner"), None),
        check_vma=False,
    )
```

```python
import jax
import jax.numpy as jnp
from jax import lax
from jax.experimental import pallas as pl
from jax.experimental.pallas import tpu as pltpu
from jax.sharding import PartitionSpec as P

H = 8
DH = 128
C = 128


def exclusive_cumsum(rows):
    running = jnp.cumsum(rows, axis=0)
    return jnp.concatenate([jnp.zeros_like(rows[:1]), running[:-1]], axis=0), running[-1]


def carried_state(local_total):
    n_inner = lax.axis_size("inner")
    n_outer = lax.axis_size("outer")
    size = local_total.size
    chunks = local_total.reshape(n_inner, size // n_inner)
    gathered = lax.all_to_all(chunks, "inner", 0, 0, tiled=True)
    inner_before, group_total = exclusive_cumsum(gathered)
    pieces = lax.all_to_all(group_total.reshape(n_outer, -1), "outer", 0, 0, tiled=True)
    outer_before, _ = exclusive_cumsum(pieces)
    outer_chunk = lax.all_to_all(outer_before, "outer", 0, 0, tiled=True).reshape(-1)
    summed = inner_before + outer_chunk[None, :]
    back = lax.all_to_all(summed, "inner", 0, 0, tiled=True)
    return back.reshape(local_total.shape)


TILE = 256
STATE_TILE = 512
INTRA_TILE = 512
PAIR = 2 * DH


def state_kernel(k_ref, v_ref, out_ref):
    @pl.when(pl.program_id(0) == 0)
    def _():
        out_ref[...] = jnp.zeros_like(out_ref)

    for h in range(H):
        cols = slice(h * DH, (h + 1) * DH)
        out_ref[h] += lax.dot_general(
            k_ref[:, cols], v_ref[:, cols], (((0,), (0,)), ((), ())),
            preferred_element_type=jnp.float32,
        )


def state_totals(keys, values):
    rows, width = keys.shape
    return pl.pallas_call(
        state_kernel,
        out_shape=jax.ShapeDtypeStruct((H, DH, DH), jnp.float32),
        grid=(rows // STATE_TILE,),
        in_specs=[
            pl.BlockSpec((STATE_TILE, width), lambda t: (t, 0)),
            pl.BlockSpec((STATE_TILE, width), lambda t: (t, 0)),
        ],
        out_specs=pl.BlockSpec((H, DH, DH), lambda t: (0, 0, 0)),
        compiler_params=pltpu.CompilerParams(dimension_semantics=("arbitrary",)),
    )(keys, values)


def intra_kernel(q_ref, k_ref, v_ref, out_ref):
    span = 2 * C
    row = lax.broadcasted_iota(jnp.int32, (span, span), 0)
    col = lax.broadcasted_iota(jnp.int32, (span, span), 1)
    causal = (row >= col) & (row // C == col // C)
    for b in range(INTRA_TILE // span):
        rows = slice(b * span, (b + 1) * span)
        for h in range(H):
            cols = slice(h * DH, (h + 1) * DH)
            scores = lax.dot_general(
                q_ref[rows, cols], k_ref[rows, cols], (((1,), (1,)), ((), ())),
                preferred_element_type=jnp.float32,
            )
            weights = jnp.where(causal, scores, 0.0).astype(jnp.bfloat16)
            out_ref[rows, cols] = jnp.dot(weights, v_ref[rows, cols], preferred_element_type=jnp.float32)


def intra_block(queries, keys, values):
    rows, width = queries.shape
    tok = lambda t: (t, 0)
    return pl.pallas_call(
        intra_kernel,
        out_shape=jax.ShapeDtypeStruct((rows, width), jnp.float32),
        grid=(rows // INTRA_TILE,),
        in_specs=[pl.BlockSpec((INTRA_TILE, width), tok)] * 3,
        out_specs=pl.BlockSpec((INTRA_TILE, width), tok),
    )(queries, keys, values)


def layer_kernel(q_ref, k_ref, v_ref, i_ref, c_ref, g_ref, w_ref, o_ref, run_ref, n_ref):
    row = lax.broadcasted_iota(jnp.int32, (PAIR, PAIR), 0)
    col = lax.broadcasted_iota(jnp.int32, (PAIR, PAIR), 1)
    same_head = row // DH == col // DH

    @pl.when(pl.program_id(0) == 0)
    def _():
        run_ref[...] = jnp.zeros_like(run_ref)
        for h in range(H):
            at = slice((h % 2) * DH, (h % 2 + 1) * DH)
            run_ref[h // 2, at, at] = c_ref[h]

    for b in range(TILE // C):
        rows = slice(b * C, (b + 1) * C)
        for p in range(H // 2):
            cols = slice(p * PAIR, (p + 1) * PAIR)
            prev = run_ref[p]
            carried_term = jnp.dot(
                q_ref[rows, cols], prev.astype(jnp.bfloat16), preferred_element_type=jnp.float32
            )
            attended = i_ref[rows, cols] + carried_term
            for half in range(2):
                part = attended[:, half * DH:(half + 1) * DH]
                mean_square = jnp.mean(part * part, axis=-1, keepdims=True)
                hcols = slice(p * PAIR + half * DH, p * PAIR + (half + 1) * DH)
                normed = part * lax.rsqrt(mean_square + 1e-06) * g_ref[:, hcols]
                n_ref[rows, hcols] = normed.astype(jnp.bfloat16)
            update = lax.dot_general(
                k_ref[rows, cols], v_ref[rows, cols], (((0,), (0,)), ((), ())),
                preferred_element_type=jnp.float32,
            )
            run_ref[p] = prev + jnp.where(same_head, update, 0.0)
    o_ref[...] = jnp.dot(n_ref[...], w_ref[...], preferred_element_type=jnp.float32).astype(
        jnp.bfloat16
    )


def layer(queries, keys, values, inside, carried, norm_gain, out_weight):
    rows, width = queries.shape
    out_width = out_weight.shape[1]
    tok = lambda t: (t, 0)
    fixed2 = lambda t: (0, 0)
    return pl.pallas_call(
        layer_kernel,
        out_shape=jax.ShapeDtypeStruct((rows, out_width), jnp.bfloat16),
        grid=(rows // TILE,),
        in_specs=[
            pl.BlockSpec((TILE, width), tok),
            pl.BlockSpec((TILE, width), tok),
            pl.BlockSpec((TILE, width), tok),
            pl.BlockSpec((TILE, width), tok),
            pl.BlockSpec((H, DH, DH), lambda t: (0, 0, 0)),
            pl.BlockSpec((1, width), fixed2),
            pl.BlockSpec((width, out_width), fixed2),
        ],
        out_specs=pl.BlockSpec((TILE, out_width), tok),
        scratch_shapes=[
            pltpu.VMEM((H // 2, PAIR, PAIR), jnp.float32),
            pltpu.VMEM((TILE, width), jnp.bfloat16),
        ],
        compiler_params=pltpu.CompilerParams(dimension_semantics=("arbitrary",)),
    )(queries, keys, values, inside, carried, norm_gain.reshape(1, width), out_weight)


def on_device(queries, keys, values, norm_gain, out_weight):
    local_total = state_totals(keys, values)
    inside = intra_block(queries, keys, values)
    carried = carried_state(local_total)
    return layer(queries, keys, values, inside, carried, norm_gain, out_weight)


def solution(mesh):
    return jax.shard_map(
        on_device,
        mesh=mesh,
        in_specs=(
            P(("outer", "inner"), None),
            P(("outer", "inner"), None),
            P(("outer", "inner"), None),
            P(),
            P(),
        ),
        out_specs=P(("outer", "inner"), None),
        check_vma=False,
    )
```

```python
import jax
import jax.numpy as jnp
from jax import lax
from jax.experimental import pallas as pl
from jax.experimental.pallas import tpu as pltpu
from jax.sharding import PartitionSpec as P

H = 8
DH = 128
C = 128


def exclusive_cumsum(rows):
    running = jnp.cumsum(rows, axis=0)
    return jnp.concatenate([jnp.zeros_like(rows[:1]), running[:-1]], axis=0), running[-1]


def carried_state(local_total):
    n_inner = lax.axis_size("inner")
    n_outer = lax.axis_size("outer")
    size = local_total.size
    chunks = local_total.reshape(n_inner, size // n_inner)
    gathered = lax.all_to_all(chunks, "inner", 0, 0, tiled=True)
    inner_before, group_total = exclusive_cumsum(gathered)
    pieces = lax.all_to_all(group_total.reshape(n_outer, -1), "outer", 0, 0, tiled=True)
    outer_before, _ = exclusive_cumsum(pieces)
    outer_chunk = lax.all_to_all(outer_before, "outer", 0, 0, tiled=True).reshape(-1)
    summed = inner_before + outer_chunk[None, :]
    back = lax.all_to_all(summed, "inner", 0, 0, tiled=True)
    return back.reshape(local_total.shape)


TILE = 256
STATE_TILE = 512
INTRA_TILE = 512
PAIR = 2 * DH


def state_kernel(k_ref, v_ref, out_ref):
    @pl.when(pl.program_id(0) == 0)
    def _():
        out_ref[...] = jnp.zeros_like(out_ref)

    for h in range(H):
        cols = slice(h * DH, (h + 1) * DH)
        out_ref[h] += lax.dot_general(
            k_ref[:, cols], v_ref[:, cols], (((0,), (0,)), ((), ())),
            preferred_element_type=jnp.float32,
        )


def state_totals(keys, values):
    rows, width = keys.shape
    return pl.pallas_call(
        state_kernel,
        out_shape=jax.ShapeDtypeStruct((H, DH, DH), jnp.float32),
        grid=(rows // STATE_TILE,),
        in_specs=[
            pl.BlockSpec((STATE_TILE, width), lambda t: (t, 0)),
            pl.BlockSpec((STATE_TILE, width), lambda t: (t, 0)),
        ],
        out_specs=pl.BlockSpec((H, DH, DH), lambda t: (0, 0, 0)),
        compiler_params=pltpu.CompilerParams(dimension_semantics=("arbitrary",)),
    )(keys, values)


def intra_kernel(q_ref, k_ref, v_ref, out_ref, within_ref, run_ref):
    span = 2 * C
    row = lax.broadcasted_iota(jnp.int32, (span, span), 0)
    col = lax.broadcasted_iota(jnp.int32, (span, span), 1)
    causal = (row >= col) & (row // C == col // C)
    for b in range(INTRA_TILE // span):
        rows = slice(b * span, (b + 1) * span)
        for h in range(H):
            cols = slice(h * DH, (h + 1) * DH)
            scores = lax.dot_general(
                q_ref[rows, cols], k_ref[rows, cols], (((1,), (1,)), ((), ())),
                preferred_element_type=jnp.float32,
            )
            weights = jnp.where(causal, scores, 0.0).astype(jnp.bfloat16)
            out_ref[rows, cols] = jnp.dot(weights, v_ref[rows, cols], preferred_element_type=jnp.float32)

    @pl.when(pl.program_id(0) == 0)
    def _():
        run_ref[...] = jnp.zeros_like(run_ref)

    for b in range(INTRA_TILE // C):
        rows = slice(b * C, (b + 1) * C)
        for h in range(H):
            cols = slice(h * DH, (h + 1) * DH)
            prev = run_ref[h]
            within_ref[b, h] = prev
            run_ref[h] = prev + lax.dot_general(
                k_ref[rows, cols], v_ref[rows, cols], (((0,), (0,)), ((), ())),
                preferred_element_type=jnp.float32,
            )


def intra_block(queries, keys, values):
    rows, width = queries.shape
    tok = lambda t: (t, 0)
    return pl.pallas_call(
        intra_kernel,
        out_shape=(
            jax.ShapeDtypeStruct((rows, width), jnp.float32),
            jax.ShapeDtypeStruct((rows // C, H, DH, DH), jnp.float32),
        ),
        grid=(rows // INTRA_TILE,),
        in_specs=[pl.BlockSpec((INTRA_TILE, width), tok)] * 3,
        out_specs=(
            pl.BlockSpec((INTRA_TILE, width), tok),
            pl.BlockSpec((INTRA_TILE // C, H, DH, DH), lambda t: (t, 0, 0, 0)),
        ),
        scratch_shapes=[pltpu.VMEM((H, DH, DH), jnp.float32)],
        compiler_params=pltpu.CompilerParams(dimension_semantics=("arbitrary",)),
    )(queries, keys, values)


def layer_kernel(q_ref, i_ref, w_in_ref, c_ref, g_ref, w_ref, o_ref, n_ref):
    for b in range(TILE // C):
        rows = slice(b * C, (b + 1) * C)
        for h in range(H):
            cols = slice(h * DH, (h + 1) * DH)
            prefix_low = (c_ref[h] + w_in_ref[b, h]).astype(jnp.bfloat16)
            carried_term = jnp.dot(q_ref[rows, cols], prefix_low, preferred_element_type=jnp.float32)
            attended = i_ref[rows, cols] + carried_term
            mean_square = jnp.mean(attended * attended, axis=-1, keepdims=True)
            normed = attended * lax.rsqrt(mean_square + 1e-06) * g_ref[:, cols]
            n_ref[rows, cols] = normed.astype(jnp.bfloat16)
    o_ref[...] = jnp.dot(n_ref[...], w_ref[...], preferred_element_type=jnp.float32).astype(
        jnp.bfloat16
    )


def layer(queries, inside, within, carried, norm_gain, out_weight):
    rows, width = queries.shape
    out_width = out_weight.shape[1]
    tok = lambda t: (t, 0)
    fixed2 = lambda t: (0, 0)
    return pl.pallas_call(
        layer_kernel,
        out_shape=jax.ShapeDtypeStruct((rows, out_width), jnp.bfloat16),
        grid=(rows // TILE,),
        in_specs=[
            pl.BlockSpec((TILE, width), tok),
            pl.BlockSpec((TILE, width), tok),
            pl.BlockSpec((TILE // C, H, DH, DH), lambda t: (t, 0, 0, 0)),
            pl.BlockSpec((H, DH, DH), lambda t: (0, 0, 0)),
            pl.BlockSpec((1, width), fixed2),
            pl.BlockSpec((width, out_width), fixed2),
        ],
        out_specs=pl.BlockSpec((TILE, out_width), tok),
        scratch_shapes=[pltpu.VMEM((TILE, width), jnp.bfloat16)],
    )(queries, inside, within, carried, norm_gain.reshape(1, width), out_weight)


def on_device(queries, keys, values, norm_gain, out_weight):
    local_total = state_totals(keys, values)
    inside, within = intra_block(queries, keys, values)
    carried = carried_state(local_total)
    return layer(queries, inside, within, carried, norm_gain, out_weight)


def solution(mesh):
    return jax.shard_map(
        on_device,
        mesh=mesh,
        in_specs=(
            P(("outer", "inner"), None),
            P(("outer", "inner"), None),
            P(("outer", "inner"), None),
            P(),
            P(),
        ),
        out_specs=P(("outer", "inner"), None),
        check_vma=False,
    )
```

```python
import jax
import jax.numpy as jnp
from jax import lax
from jax.experimental import pallas as pl
from jax.experimental.pallas import tpu as pltpu
from jax.sharding import PartitionSpec as P

H = 8
DH = 128
C = 128


def exclusive_cumsum(rows):
    running = jnp.cumsum(rows, axis=0)
    return jnp.concatenate([jnp.zeros_like(rows[:1]), running[:-1]], axis=0), running[-1]


def carried_state(local_total):
    n_inner = lax.axis_size("inner")
    n_outer = lax.axis_size("outer")
    lanes = local_total.shape[-1]
    chunks = local_total.reshape(n_inner, -1, lanes)
    gathered = lax.all_to_all(chunks, "inner", 0, 0, tiled=False)
    inner_before, group_total = exclusive_cumsum(gathered)
    pieces = lax.all_to_all(group_total.reshape(n_outer, -1, lanes), "outer", 0, 0, tiled=False)
    outer_before, _ = exclusive_cumsum(pieces)
    outer_chunk = lax.all_to_all(outer_before, "outer", 0, 0, tiled=False)
    summed = inner_before + outer_chunk.reshape(1, -1, lanes)
    back = lax.all_to_all(summed, "inner", 0, 0, tiled=False)
    return back.reshape(local_total.shape)


TILE = 256
STATE_TILE = 512
INTRA_TILE = 512
PAIR = 2 * DH


def state_kernel(k_ref, v_ref, out_ref):
    @pl.when(pl.program_id(0) == 0)
    def _():
        out_ref[...] = jnp.zeros_like(out_ref)

    for h in range(H):
        cols = slice(h * DH, (h + 1) * DH)
        out_ref[h] += lax.dot_general(
            k_ref[:, cols], v_ref[:, cols], (((0,), (0,)), ((), ())),
            preferred_element_type=jnp.float32,
        )


def state_totals(keys, values):
    rows, width = keys.shape
    return pl.pallas_call(
        state_kernel,
        out_shape=jax.ShapeDtypeStruct((H, DH, DH), jnp.float32),
        grid=(rows // STATE_TILE,),
        in_specs=[
            pl.BlockSpec((STATE_TILE, width), lambda t: (t, 0)),
            pl.BlockSpec((STATE_TILE, width), lambda t: (t, 0)),
        ],
        out_specs=pl.BlockSpec((H, DH, DH), lambda t: (0, 0, 0)),
        compiler_params=pltpu.CompilerParams(dimension_semantics=("arbitrary",)),
    )(keys, values)


def intra_kernel(q_ref, k_ref, v_ref, out_ref, within_ref, run_ref):
    span = 2 * C
    row = lax.broadcasted_iota(jnp.int32, (span, span), 0)
    col = lax.broadcasted_iota(jnp.int32, (span, span), 1)
    causal = (row >= col) & (row // C == col // C)
    for b in range(INTRA_TILE // span):
        rows = slice(b * span, (b + 1) * span)
        for h in range(H):
            cols = slice(h * DH, (h + 1) * DH)
            scores = lax.dot_general(
                q_ref[rows, cols], k_ref[rows, cols], (((1,), (1,)), ((), ())),
                preferred_element_type=jnp.float32,
            )
            weights = jnp.where(causal, scores, 0.0).astype(jnp.bfloat16)
            out_ref[rows, cols] = jnp.dot(weights, v_ref[rows, cols], preferred_element_type=jnp.float32)

    @pl.when(pl.program_id(0) == 0)
    def _():
        run_ref[...] = jnp.zeros_like(run_ref)

    for b in range(INTRA_TILE // C):
        rows = slice(b * C, (b + 1) * C)
        for h in range(H):
            cols = slice(h * DH, (h + 1) * DH)
            prev = run_ref[h]
            within_ref[b, h] = prev
            run_ref[h] = prev + lax.dot_general(
                k_ref[rows, cols], v_ref[rows, cols], (((0,), (0,)), ((), ())),
                preferred_element_type=jnp.float32,
            )


def intra_block(queries, keys, values):
    rows, width = queries.shape
    tok = lambda t: (t, 0)
    return pl.pallas_call(
        intra_kernel,
        out_shape=(
            jax.ShapeDtypeStruct((rows, width), jnp.float32),
            jax.ShapeDtypeStruct((rows // C, H, DH, DH), jnp.float32),
        ),
        grid=(rows // INTRA_TILE,),
        in_specs=[pl.BlockSpec((INTRA_TILE, width), tok)] * 3,
        out_specs=(
            pl.BlockSpec((INTRA_TILE, width), tok),
            pl.BlockSpec((INTRA_TILE // C, H, DH, DH), lambda t: (t, 0, 0, 0)),
        ),
        scratch_shapes=[pltpu.VMEM((H, DH, DH), jnp.float32)],
        compiler_params=pltpu.CompilerParams(dimension_semantics=("arbitrary",)),
    )(queries, keys, values)


def layer_kernel(q_ref, i_ref, w_in_ref, c_ref, g_ref, w_ref, o_ref, n_ref):
    for b in range(TILE // C):
        rows = slice(b * C, (b + 1) * C)
        for h in range(H):
            cols = slice(h * DH, (h + 1) * DH)
            prefix_low = (c_ref[h] + w_in_ref[b, h]).astype(jnp.bfloat16)
            carried_term = jnp.dot(q_ref[rows, cols], prefix_low, preferred_element_type=jnp.float32)
            attended = i_ref[rows, cols] + carried_term
            mean_square = jnp.mean(attended * attended, axis=-1, keepdims=True)
            normed = attended * lax.rsqrt(mean_square + 1e-06) * g_ref[:, cols]
            n_ref[rows, cols] = normed.astype(jnp.bfloat16)
    o_ref[...] = jnp.dot(n_ref[...], w_ref[...], preferred_element_type=jnp.float32).astype(
        jnp.bfloat16
    )


def layer(queries, inside, within, carried, norm_gain, out_weight):
    rows, width = queries.shape
    out_width = out_weight.shape[1]
    tok = lambda t: (t, 0)
    fixed2 = lambda t: (0, 0)
    return pl.pallas_call(
        layer_kernel,
        out_shape=jax.ShapeDtypeStruct((rows, out_width), jnp.bfloat16),
        grid=(rows // TILE,),
        in_specs=[
            pl.BlockSpec((TILE, width), tok),
            pl.BlockSpec((TILE, width), tok),
            pl.BlockSpec((TILE // C, H, DH, DH), lambda t: (t, 0, 0, 0)),
            pl.BlockSpec((H, DH, DH), lambda t: (0, 0, 0)),
            pl.BlockSpec((1, width), fixed2),
            pl.BlockSpec((width, out_width), fixed2),
        ],
        out_specs=pl.BlockSpec((TILE, out_width), tok),
        scratch_shapes=[pltpu.VMEM((TILE, width), jnp.bfloat16)],
    )(queries, inside, within, carried, norm_gain.reshape(1, width), out_weight)


def on_device(queries, keys, values, norm_gain, out_weight):
    local_total = state_totals(keys, values)
    inside, within = intra_block(queries, keys, values)
    carried = carried_state(local_total)
    return layer(queries, inside, within, carried, norm_gain, out_weight)


def solution(mesh):
    return jax.shard_map(
        on_device,
        mesh=mesh,
        in_specs=(
            P(("outer", "inner"), None),
            P(("outer", "inner"), None),
            P(("outer", "inner"), None),
            P(),
            P(),
        ),
        out_specs=P(("outer", "inner"), None),
        check_vma=False,
    )
```

```python
import jax
import jax.numpy as jnp
from jax import lax
from jax.experimental import pallas as pl
from jax.experimental.pallas import tpu as pltpu
from jax.sharding import PartitionSpec as P

H = 8
DH = 128
C = 128


def exclusive_cumsum(rows):
    running = jnp.cumsum(rows, axis=0)
    return jnp.concatenate([jnp.zeros_like(rows[:1]), running[:-1]], axis=0), running[-1]


def carried_state(local_total):
    n_inner = lax.axis_size("inner")
    n_outer = lax.axis_size("outer")
    lanes = local_total.shape[-1]
    chunks = local_total.reshape(n_inner, -1, lanes)
    gathered = lax.all_to_all(chunks, "inner", 0, 0, tiled=False)
    inner_before, group_total = exclusive_cumsum(gathered)
    pieces = lax.all_to_all(group_total.reshape(n_outer, -1, lanes), "outer", 0, 0, tiled=False)
    outer_before, _ = exclusive_cumsum(pieces)
    outer_chunk = lax.all_to_all(outer_before, "outer", 0, 0, tiled=False)
    summed = inner_before + outer_chunk.reshape(1, -1, lanes)
    back = lax.all_to_all(summed, "inner", 0, 0, tiled=False)
    return back.reshape(local_total.shape)


TILE = 256
STATE_TILE = 512
INTRA_TILE = 512
PAIR = 2 * DH


def state_kernel(k_ref, v_ref, out_ref):
    @pl.when(pl.program_id(0) == 0)
    def _():
        out_ref[...] = jnp.zeros_like(out_ref)

    for h in range(H):
        cols = slice(h * DH, (h + 1) * DH)
        out_ref[h] += lax.dot_general(
            k_ref[:, cols], v_ref[:, cols], (((0,), (0,)), ((), ())),
            preferred_element_type=jnp.float32,
        )


def state_totals(keys, values):
    rows, width = keys.shape
    return pl.pallas_call(
        state_kernel,
        out_shape=jax.ShapeDtypeStruct((H, DH, DH), jnp.float32),
        grid=(rows // STATE_TILE,),
        in_specs=[
            pl.BlockSpec((STATE_TILE, width), lambda t: (t, 0)),
            pl.BlockSpec((STATE_TILE, width), lambda t: (t, 0)),
        ],
        out_specs=pl.BlockSpec((H, DH, DH), lambda t: (0, 0, 0)),
        compiler_params=pltpu.CompilerParams(dimension_semantics=("arbitrary",)),
    )(keys, values)


def intra_kernel(q_ref, k_ref, v_ref, out_ref, within_ref, run_ref):
    span = 2 * C
    row = lax.broadcasted_iota(jnp.int32, (span, span), 0)
    col = lax.broadcasted_iota(jnp.int32, (span, span), 1)
    causal = (row >= col) & (row // C == col // C)
    for b in range(INTRA_TILE // span):
        rows = slice(b * span, (b + 1) * span)
        for h in range(H):
            cols = slice(h * DH, (h + 1) * DH)
            scores = lax.dot_general(
                q_ref[rows, cols], k_ref[rows, cols], (((1,), (1,)), ((), ())),
                preferred_element_type=jnp.float32,
            )
            weights = jnp.where(causal, scores, 0.0).astype(jnp.bfloat16)
            out_ref[rows, cols] = jnp.dot(weights, v_ref[rows, cols], preferred_element_type=jnp.float32)

    @pl.when(pl.program_id(0) == 0)
    def _():
        run_ref[...] = jnp.zeros_like(run_ref)

    for b in range(INTRA_TILE // C):
        rows = slice(b * C, (b + 1) * C)
        for h in range(H):
            cols = slice(h * DH, (h + 1) * DH)
            prev = run_ref[h]
            within_ref[b, h] = prev
            run_ref[h] = prev + lax.dot_general(
                k_ref[rows, cols], v_ref[rows, cols], (((0,), (0,)), ((), ())),
                preferred_element_type=jnp.float32,
            )


def intra_block(queries, keys, values):
    rows, width = queries.shape
    tok = lambda t: (t, 0)
    return pl.pallas_call(
        intra_kernel,
        out_shape=(
            jax.ShapeDtypeStruct((rows, width), jnp.float32),
            jax.ShapeDtypeStruct((rows // C, H, DH, DH), jnp.float32),
        ),
        grid=(rows // INTRA_TILE,),
        in_specs=[pl.BlockSpec((INTRA_TILE, width), tok)] * 3,
        out_specs=(
            pl.BlockSpec((INTRA_TILE, width), tok),
            pl.BlockSpec((INTRA_TILE // C, H, DH, DH), lambda t: (t, 0, 0, 0)),
        ),
        scratch_shapes=[pltpu.VMEM((H, DH, DH), jnp.float32)],
        compiler_params=pltpu.CompilerParams(dimension_semantics=("arbitrary",)),
    )(queries, keys, values)


WEIGHT_PARTS = 4


def layer_kernel(q_ref, i_ref, w_in_ref, c_ref, g_ref, w_hbm, o_ref, n_ref, w_ref, sems):
    first = pl.program_id(0) == 0
    rows_part = w_ref.shape[0] // WEIGHT_PARTS

    def weight_copy(j):
        part = pl.ds(j * rows_part, rows_part)
        return pltpu.make_async_copy(w_hbm.at[part, :], w_ref.at[part, :], sems.at[j])

    @pl.when(first)
    def _():
        for j in range(WEIGHT_PARTS):
            weight_copy(j).start()

    for b in range(TILE // C):
        rows = slice(b * C, (b + 1) * C)
        for h in range(H):
            cols = slice(h * DH, (h + 1) * DH)
            prefix_low = (c_ref[h] + w_in_ref[b, h]).astype(jnp.bfloat16)
            carried_term = jnp.dot(q_ref[rows, cols], prefix_low, preferred_element_type=jnp.float32)
            attended = i_ref[rows, cols] + carried_term
            mean_square = jnp.mean(attended * attended, axis=-1, keepdims=True)
            normed = attended * lax.rsqrt(mean_square + 1e-06) * g_ref[:, cols]
            n_ref[rows, cols] = normed.astype(jnp.bfloat16)
    total = None
    for j in range(WEIGHT_PARTS):
        @pl.when(first)
        def _():
            weight_copy(j).wait()

        part = slice(j * rows_part, (j + 1) * rows_part)
        piece = jnp.dot(n_ref[:, part], w_ref[part, :], preferred_element_type=jnp.float32)
        total = piece if total is None else total + piece
    o_ref[...] = total.astype(jnp.bfloat16)


def layer(queries, inside, within, carried, norm_gain, out_weight):
    rows, width = queries.shape
    out_width = out_weight.shape[1]
    tok = lambda t: (t, 0)
    fixed2 = lambda t: (0, 0)
    return pl.pallas_call(
        layer_kernel,
        out_shape=jax.ShapeDtypeStruct((rows, out_width), jnp.bfloat16),
        grid=(rows // TILE,),
        in_specs=[
            pl.BlockSpec((TILE, width), tok),
            pl.BlockSpec((TILE, width), tok),
            pl.BlockSpec((TILE // C, H, DH, DH), lambda t: (t, 0, 0, 0)),
            pl.BlockSpec((H, DH, DH), lambda t: (0, 0, 0)),
            pl.BlockSpec((1, width), fixed2),
            pl.BlockSpec(memory_space=pl.ANY),
        ],
        out_specs=pl.BlockSpec((TILE, out_width), tok),
        scratch_shapes=[
            pltpu.VMEM((TILE, width), jnp.bfloat16),
            pltpu.VMEM((width, out_width), jnp.bfloat16),
            pltpu.SemaphoreType.DMA((WEIGHT_PARTS,)),
        ],
        compiler_params=pltpu.CompilerParams(dimension_semantics=("arbitrary",)),
    )(queries, inside, within, carried, norm_gain.reshape(1, width), out_weight)


def on_device(queries, keys, values, norm_gain, out_weight):
    local_total = state_totals(keys, values)
    inside, within = intra_block(queries, keys, values)
    carried = carried_state(local_total)
    return layer(queries, inside, within, carried, norm_gain, out_weight)


def solution(mesh):
    return jax.shard_map(
        on_device,
        mesh=mesh,
        in_specs=(
            P(("outer", "inner"), None),
            P(("outer", "inner"), None),
            P(("outer", "inner"), None),
            P(),
            P(),
        ),
        out_specs=P(("outer", "inner"), None),
        check_vma=False,
    )
```

```python
import jax
import jax.numpy as jnp
from jax import lax
from jax.experimental import pallas as pl
from jax.experimental.pallas import tpu as pltpu
from jax.sharding import PartitionSpec as P

H = 8
DH = 128
C = 128


def exclusive_cumsum(rows):
    running = jnp.cumsum(rows, axis=0)
    return jnp.concatenate([jnp.zeros_like(rows[:1]), running[:-1]], axis=0), running[-1]


def carried_state(local_total):
    axes = ("outer", "inner")
    devices = lax.axis_size(axes)
    lanes = local_total.shape[-1]
    pieces = local_total.reshape(devices, -1, lanes)
    gathered = lax.all_to_all(pieces, axes, 0, 0, tiled=False)
    n_inner = lax.axis_size("inner")
    groups = gathered.reshape(devices // n_inner, n_inner, -1, lanes)
    running = jnp.cumsum(groups, axis=1)
    inner_before = jnp.concatenate([jnp.zeros_like(running[:, :1]), running[:, :-1]], axis=1)
    outer_before, _ = exclusive_cumsum(running[:, -1])
    before = (inner_before + outer_before[:, None]).reshape(gathered.shape)
    back = lax.all_to_all(before, axes, 0, 0, tiled=False)
    return back.reshape(local_total.shape)


TILE = 256
STATE_TILE = 512
INTRA_TILE = 512
PAIR = 2 * DH


def state_kernel(k_ref, v_ref, out_ref):
    @pl.when(pl.program_id(0) == 0)
    def _():
        out_ref[...] = jnp.zeros_like(out_ref)

    for h in range(H):
        cols = slice(h * DH, (h + 1) * DH)
        out_ref[h] += lax.dot_general(
            k_ref[:, cols], v_ref[:, cols], (((0,), (0,)), ((), ())),
            preferred_element_type=jnp.float32,
        )


def state_totals(keys, values):
    rows, width = keys.shape
    return pl.pallas_call(
        state_kernel,
        out_shape=jax.ShapeDtypeStruct((H, DH, DH), jnp.float32),
        grid=(rows // STATE_TILE,),
        in_specs=[
            pl.BlockSpec((STATE_TILE, width), lambda t: (t, 0)),
            pl.BlockSpec((STATE_TILE, width), lambda t: (t, 0)),
        ],
        out_specs=pl.BlockSpec((H, DH, DH), lambda t: (0, 0, 0)),
        compiler_params=pltpu.CompilerParams(dimension_semantics=("arbitrary",)),
    )(keys, values)


def intra_kernel(q_ref, k_ref, v_ref, out_ref, within_ref, run_ref):
    span = 2 * C
    row = lax.broadcasted_iota(jnp.int32, (span, span), 0)
    col = lax.broadcasted_iota(jnp.int32, (span, span), 1)
    causal = (row >= col) & (row // C == col // C)
    for b in range(INTRA_TILE // span):
        rows = slice(b * span, (b + 1) * span)
        for h in range(H):
            cols = slice(h * DH, (h + 1) * DH)
            scores = lax.dot_general(
                q_ref[rows, cols], k_ref[rows, cols], (((1,), (1,)), ((), ())),
                preferred_element_type=jnp.float32,
            )
            weights = jnp.where(causal, scores, 0.0).astype(jnp.bfloat16)
            out_ref[rows, cols] = jnp.dot(weights, v_ref[rows, cols], preferred_element_type=jnp.float32)

    @pl.when(pl.program_id(0) == 0)
    def _():
        run_ref[...] = jnp.zeros_like(run_ref)

    for b in range(INTRA_TILE // C):
        rows = slice(b * C, (b + 1) * C)
        for h in range(H):
            cols = slice(h * DH, (h + 1) * DH)
            prev = run_ref[h]
            within_ref[b, h] = prev
            run_ref[h] = prev + lax.dot_general(
                k_ref[rows, cols], v_ref[rows, cols], (((0,), (0,)), ((), ())),
                preferred_element_type=jnp.float32,
            )


def intra_block(queries, keys, values):
    rows, width = queries.shape
    tok = lambda t: (t, 0)
    return pl.pallas_call(
        intra_kernel,
        out_shape=(
            jax.ShapeDtypeStruct((rows, width), jnp.float32),
            jax.ShapeDtypeStruct((rows // C, H, DH, DH), jnp.float32),
        ),
        grid=(rows // INTRA_TILE,),
        in_specs=[pl.BlockSpec((INTRA_TILE, width), tok)] * 3,
        out_specs=(
            pl.BlockSpec((INTRA_TILE, width), tok),
            pl.BlockSpec((INTRA_TILE // C, H, DH, DH), lambda t: (t, 0, 0, 0)),
        ),
        scratch_shapes=[pltpu.VMEM((H, DH, DH), jnp.float32)],
        compiler_params=pltpu.CompilerParams(dimension_semantics=("arbitrary",)),
    )(queries, keys, values)


def layer_kernel(q_ref, i_ref, w_in_ref, c_ref, g_ref, w_ref, o_ref, n_ref):
    for b in range(TILE // C):
        rows = slice(b * C, (b + 1) * C)
        for h in range(H):
            cols = slice(h * DH, (h + 1) * DH)
            prefix_low = (c_ref[h] + w_in_ref[b, h]).astype(jnp.bfloat16)
            carried_term = jnp.dot(q_ref[rows, cols], prefix_low, preferred_element_type=jnp.float32)
            attended = i_ref[rows, cols] + carried_term
            mean_square = jnp.mean(attended * attended, axis=-1, keepdims=True)
            normed = attended * lax.rsqrt(mean_square + 1e-06) * g_ref[:, cols]
            n_ref[rows, cols] = normed.astype(jnp.bfloat16)
    o_ref[...] = jnp.dot(n_ref[...], w_ref[...], preferred_element_type=jnp.float32).astype(
        jnp.bfloat16
    )


def layer(queries, inside, within, carried, norm_gain, out_weight):
    rows, width = queries.shape
    out_width = out_weight.shape[1]
    tok = lambda t: (t, 0)
    fixed2 = lambda t: (0, 0)
    return pl.pallas_call(
        layer_kernel,
        out_shape=jax.ShapeDtypeStruct((rows, out_width), jnp.bfloat16),
        grid=(rows // TILE,),
        in_specs=[
            pl.BlockSpec((TILE, width), tok),
            pl.BlockSpec((TILE, width), tok),
            pl.BlockSpec((TILE // C, H, DH, DH), lambda t: (t, 0, 0, 0)),
            pl.BlockSpec((H, DH, DH), lambda t: (0, 0, 0)),
            pl.BlockSpec((1, width), fixed2),
            pl.BlockSpec((width, out_width), fixed2),
        ],
        out_specs=pl.BlockSpec((TILE, out_width), tok),
        scratch_shapes=[pltpu.VMEM((TILE, width), jnp.bfloat16)],
    )(queries, inside, within, carried, norm_gain.reshape(1, width), out_weight)


def on_device(queries, keys, values, norm_gain, out_weight):
    local_total = state_totals(keys, values)
    inside, within = intra_block(queries, keys, values)
    carried = carried_state(local_total)
    return layer(queries, inside, within, carried, norm_gain, out_weight)


def solution(mesh):
    return jax.shard_map(
        on_device,
        mesh=mesh,
        in_specs=(
            P(("outer", "inner"), None),
            P(("outer", "inner"), None),
            P(("outer", "inner"), None),
            P(),
            P(),
        ),
        out_specs=P(("outer", "inner"), None),
        check_vma=False,
    )
```

```python
import jax
import jax.numpy as jnp
from jax import lax
from jax.experimental import pallas as pl
from jax.experimental.pallas import tpu as pltpu
from jax.sharding import PartitionSpec as P

H = 8
DH = 128
C = 128


def exclusive_cumsum(rows):
    running = jnp.cumsum(rows, axis=0)
    return jnp.concatenate([jnp.zeros_like(rows[:1]), running[:-1]], axis=0), running[-1]


def carried_state(local_total):
    axes = ("outer", "inner")
    devices = lax.axis_size(axes)
    lanes = local_total.shape[-1]
    pieces = local_total.reshape(devices, -1, lanes)
    gathered = lax.all_to_all(pieces, axes, 0, 0, tiled=False)
    earlier = lax.broadcasted_iota(jnp.int32, (devices, devices), 0) > lax.broadcasted_iota(
        jnp.int32, (devices, devices), 1
    )
    before = jnp.dot(
        earlier.astype(jnp.float32), gathered.reshape(devices, -1),
        precision=lax.Precision.HIGHEST, preferred_element_type=jnp.float32,
    ).reshape(gathered.shape)
    back = lax.all_to_all(before, axes, 0, 0, tiled=False)
    return back.reshape(local_total.shape)


TILE = 256
STATE_TILE = 512
INTRA_TILE = 512
PAIR = 2 * DH


def state_kernel(k_ref, v_ref, out_ref):
    @pl.when(pl.program_id(0) == 0)
    def _():
        out_ref[...] = jnp.zeros_like(out_ref)

    for h in range(H):
        cols = slice(h * DH, (h + 1) * DH)
        out_ref[h] += lax.dot_general(
            k_ref[:, cols], v_ref[:, cols], (((0,), (0,)), ((), ())),
            preferred_element_type=jnp.float32,
        )


def state_totals(keys, values):
    rows, width = keys.shape
    return pl.pallas_call(
        state_kernel,
        out_shape=jax.ShapeDtypeStruct((H, DH, DH), jnp.float32),
        grid=(rows // STATE_TILE,),
        in_specs=[
            pl.BlockSpec((STATE_TILE, width), lambda t: (t, 0)),
            pl.BlockSpec((STATE_TILE, width), lambda t: (t, 0)),
        ],
        out_specs=pl.BlockSpec((H, DH, DH), lambda t: (0, 0, 0)),
        compiler_params=pltpu.CompilerParams(dimension_semantics=("arbitrary",)),
    )(keys, values)


def intra_kernel(q_ref, k_ref, v_ref, out_ref, within_ref, run_ref):
    span = 2 * C
    row = lax.broadcasted_iota(jnp.int32, (span, span), 0)
    col = lax.broadcasted_iota(jnp.int32, (span, span), 1)
    causal = (row >= col) & (row // C == col // C)
    for b in range(INTRA_TILE // span):
        rows = slice(b * span, (b + 1) * span)
        for h in range(H):
            cols = slice(h * DH, (h + 1) * DH)
            scores = lax.dot_general(
                q_ref[rows, cols], k_ref[rows, cols], (((1,), (1,)), ((), ())),
                preferred_element_type=jnp.float32,
            )
            weights = jnp.where(causal, scores, 0.0).astype(jnp.bfloat16)
            out_ref[rows, cols] = jnp.dot(weights, v_ref[rows, cols], preferred_element_type=jnp.float32)

    @pl.when(pl.program_id(0) == 0)
    def _():
        run_ref[...] = jnp.zeros_like(run_ref)

    for b in range(INTRA_TILE // C):
        rows = slice(b * C, (b + 1) * C)
        for h in range(H):
            cols = slice(h * DH, (h + 1) * DH)
            prev = run_ref[h]
            within_ref[b, h] = prev
            run_ref[h] = prev + lax.dot_general(
                k_ref[rows, cols], v_ref[rows, cols], (((0,), (0,)), ((), ())),
                preferred_element_type=jnp.float32,
            )


def intra_block(queries, keys, values):
    rows, width = queries.shape
    tok = lambda t: (t, 0)
    return pl.pallas_call(
        intra_kernel,
        out_shape=(
            jax.ShapeDtypeStruct((rows, width), jnp.float32),
            jax.ShapeDtypeStruct((rows // C, H, DH, DH), jnp.float32),
        ),
        grid=(rows // INTRA_TILE,),
        in_specs=[pl.BlockSpec((INTRA_TILE, width), tok)] * 3,
        out_specs=(
            pl.BlockSpec((INTRA_TILE, width), tok),
            pl.BlockSpec((INTRA_TILE // C, H, DH, DH), lambda t: (t, 0, 0, 0)),
        ),
        scratch_shapes=[pltpu.VMEM((H, DH, DH), jnp.float32)],
        compiler_params=pltpu.CompilerParams(dimension_semantics=("arbitrary",)),
    )(queries, keys, values)


def layer_kernel(q_ref, i_ref, w_in_ref, c_ref, g_ref, w_ref, o_ref, n_ref):
    for b in range(TILE // C):
        rows = slice(b * C, (b + 1) * C)
        for h in range(H):
            cols = slice(h * DH, (h + 1) * DH)
            prefix_low = (c_ref[h] + w_in_ref[b, h]).astype(jnp.bfloat16)
            carried_term = jnp.dot(q_ref[rows, cols], prefix_low, preferred_element_type=jnp.float32)
            attended = i_ref[rows, cols] + carried_term
            mean_square = jnp.mean(attended * attended, axis=-1, keepdims=True)
            normed = attended * lax.rsqrt(mean_square + 1e-06) * g_ref[:, cols]
            n_ref[rows, cols] = normed.astype(jnp.bfloat16)
    o_ref[...] = jnp.dot(n_ref[...], w_ref[...], preferred_element_type=jnp.float32).astype(
        jnp.bfloat16
    )


def layer(queries, inside, within, carried, norm_gain, out_weight):
    rows, width = queries.shape
    out_width = out_weight.shape[1]
    tok = lambda t: (t, 0)
    fixed2 = lambda t: (0, 0)
    return pl.pallas_call(
        layer_kernel,
        out_shape=jax.ShapeDtypeStruct((rows, out_width), jnp.bfloat16),
        grid=(rows // TILE,),
        in_specs=[
            pl.BlockSpec((TILE, width), tok),
            pl.BlockSpec((TILE, width), tok),
            pl.BlockSpec((TILE // C, H, DH, DH), lambda t: (t, 0, 0, 0)),
            pl.BlockSpec((H, DH, DH), lambda t: (0, 0, 0)),
            pl.BlockSpec((1, width), fixed2),
            pl.BlockSpec((width, out_width), fixed2),
        ],
        out_specs=pl.BlockSpec((TILE, out_width), tok),
        scratch_shapes=[pltpu.VMEM((TILE, width), jnp.bfloat16)],
    )(queries, inside, within, carried, norm_gain.reshape(1, width), out_weight)


def on_device(queries, keys, values, norm_gain, out_weight):
    local_total = state_totals(keys, values)
    inside, within = intra_block(queries, keys, values)
    carried = carried_state(local_total)
    return layer(queries, inside, within, carried, norm_gain, out_weight)


def solution(mesh):
    return jax.shard_map(
        on_device,
        mesh=mesh,
        in_specs=(
            P(("outer", "inner"), None),
            P(("outer", "inner"), None),
            P(("outer", "inner"), None),
            P(),
            P(),
        ),
        out_specs=P(("outer", "inner"), None),
        check_vma=False,
    )
```

```python
import jax
import jax.numpy as jnp
from jax import lax
from jax.experimental import pallas as pl
from jax.experimental.pallas import tpu as pltpu
from jax.sharding import PartitionSpec as P

H = 8
DH = 128
C = 128


def exclusive_cumsum(rows):
    running = jnp.cumsum(rows, axis=0)
    return jnp.concatenate([jnp.zeros_like(rows[:1]), running[:-1]], axis=0), running[-1]


def carried_state(local_total, held):
    axes = ("outer", "inner")
    devices = lax.axis_size(axes)
    lanes = local_total.shape[-1]
    pieces = local_total.reshape(devices, -1, lanes)
    gathered = lax.all_to_all(pieces, axes, 0, 0, tiled=False)
    earlier = lax.broadcasted_iota(jnp.int32, (devices, devices), 0) > lax.broadcasted_iota(
        jnp.int32, (devices, devices), 1
    )
    before = jnp.dot(
        earlier.astype(jnp.float32), gathered.reshape(devices, -1),
        precision=lax.Precision.HIGHEST, preferred_element_type=jnp.float32,
    ).reshape(gathered.shape)
    before, held = lax.optimization_barrier((before, held))
    back = lax.all_to_all(before, axes, 0, 0, tiled=False)
    return back.reshape(local_total.shape), held


TILE = 256
STATE_TILE = 512
INTRA_TILE = 512
PAIR = 2 * DH


def state_kernel(k_ref, v_ref, out_ref):
    @pl.when(pl.program_id(0) == 0)
    def _():
        out_ref[...] = jnp.zeros_like(out_ref)

    for h in range(H):
        cols = slice(h * DH, (h + 1) * DH)
        out_ref[h] += lax.dot_general(
            k_ref[:, cols], v_ref[:, cols], (((0,), (0,)), ((), ())),
            preferred_element_type=jnp.float32,
        )


def state_totals(keys, values):
    rows, width = keys.shape
    return pl.pallas_call(
        state_kernel,
        out_shape=jax.ShapeDtypeStruct((H, DH, DH), jnp.float32),
        grid=(rows // STATE_TILE,),
        in_specs=[
            pl.BlockSpec((STATE_TILE, width), lambda t: (t, 0)),
            pl.BlockSpec((STATE_TILE, width), lambda t: (t, 0)),
        ],
        out_specs=pl.BlockSpec((H, DH, DH), lambda t: (0, 0, 0)),
        compiler_params=pltpu.CompilerParams(dimension_semantics=("arbitrary",)),
    )(keys, values)


def intra_kernel(q_ref, k_ref, v_ref, out_ref, within_ref, run_ref):
    span = 2 * C
    row = lax.broadcasted_iota(jnp.int32, (span, span), 0)
    col = lax.broadcasted_iota(jnp.int32, (span, span), 1)
    causal = (row >= col) & (row // C == col // C)
    for b in range(INTRA_TILE // span):
        rows = slice(b * span, (b + 1) * span)
        for h in range(H):
            cols = slice(h * DH, (h + 1) * DH)
            scores = lax.dot_general(
                q_ref[rows, cols], k_ref[rows, cols], (((1,), (1,)), ((), ())),
                preferred_element_type=jnp.float32,
            )
            weights = jnp.where(causal, scores, 0.0).astype(jnp.bfloat16)
            out_ref[rows, cols] = jnp.dot(weights, v_ref[rows, cols], preferred_element_type=jnp.float32)

    @pl.when(pl.program_id(0) == 0)
    def _():
        run_ref[...] = jnp.zeros_like(run_ref)

    for b in range(INTRA_TILE // C):
        rows = slice(b * C, (b + 1) * C)
        for h in range(H):
            cols = slice(h * DH, (h + 1) * DH)
            prev = run_ref[h]
            within_ref[b, h] = prev
            run_ref[h] = prev + lax.dot_general(
                k_ref[rows, cols], v_ref[rows, cols], (((0,), (0,)), ((), ())),
                preferred_element_type=jnp.float32,
            )


def intra_block(queries, keys, values):
    rows, width = queries.shape
    tok = lambda t: (t, 0)
    return pl.pallas_call(
        intra_kernel,
        out_shape=(
            jax.ShapeDtypeStruct((rows, width), jnp.float32),
            jax.ShapeDtypeStruct((rows // C, H, DH, DH), jnp.float32),
        ),
        grid=(rows // INTRA_TILE,),
        in_specs=[pl.BlockSpec((INTRA_TILE, width), tok)] * 3,
        out_specs=(
            pl.BlockSpec((INTRA_TILE, width), tok),
            pl.BlockSpec((INTRA_TILE // C, H, DH, DH), lambda t: (t, 0, 0, 0)),
        ),
        scratch_shapes=[pltpu.VMEM((H, DH, DH), jnp.float32)],
        compiler_params=pltpu.CompilerParams(dimension_semantics=("arbitrary",)),
    )(queries, keys, values)


def layer_kernel(q_ref, i_ref, w_in_ref, c_ref, g_ref, w_ref, o_ref, n_ref):
    for b in range(TILE // C):
        rows = slice(b * C, (b + 1) * C)
        for h in range(H):
            cols = slice(h * DH, (h + 1) * DH)
            prefix_low = (c_ref[h] + w_in_ref[b, h]).astype(jnp.bfloat16)
            carried_term = jnp.dot(q_ref[rows, cols], prefix_low, preferred_element_type=jnp.float32)
            attended = i_ref[rows, cols] + carried_term
            mean_square = jnp.mean(attended * attended, axis=-1, keepdims=True)
            normed = attended * lax.rsqrt(mean_square + 1e-06) * g_ref[:, cols]
            n_ref[rows, cols] = normed.astype(jnp.bfloat16)
    o_ref[...] = jnp.dot(n_ref[...], w_ref[...], preferred_element_type=jnp.float32).astype(
        jnp.bfloat16
    )


def layer(queries, inside, within, carried, norm_gain, out_weight):
    rows, width = queries.shape
    out_width = out_weight.shape[1]
    tok = lambda t: (t, 0)
    fixed2 = lambda t: (0, 0)
    return pl.pallas_call(
        layer_kernel,
        out_shape=jax.ShapeDtypeStruct((rows, out_width), jnp.bfloat16),
        grid=(rows // TILE,),
        in_specs=[
            pl.BlockSpec((TILE, width), tok),
            pl.BlockSpec((TILE, width), tok),
            pl.BlockSpec((TILE // C, H, DH, DH), lambda t: (t, 0, 0, 0)),
            pl.BlockSpec((H, DH, DH), lambda t: (0, 0, 0)),
            pl.BlockSpec((1, width), fixed2),
            pl.BlockSpec((width, out_width), fixed2),
        ],
        out_specs=pl.BlockSpec((TILE, out_width), tok),
        scratch_shapes=[pltpu.VMEM((TILE, width), jnp.bfloat16)],
    )(queries, inside, within, carried, norm_gain.reshape(1, width), out_weight)


def on_device(queries, keys, values, norm_gain, out_weight):
    local_total = state_totals(keys, values)
    carried, (inside, within) = carried_state(local_total, intra_block(queries, keys, values))
    return layer(queries, inside, within, carried, norm_gain, out_weight)


def solution(mesh):
    return jax.shard_map(
        on_device,
        mesh=mesh,
        in_specs=(
            P(("outer", "inner"), None),
            P(("outer", "inner"), None),
            P(("outer", "inner"), None),
            P(),
            P(),
        ),
        out_specs=P(("outer", "inner"), None),
        check_vma=False,
    )
```
